256 devices in a mesh: gx: 8 (over y, core), gy: 8 (over z), ba: 4 (over x).
Axes of the slice: x: 4, y: 4, z: 8, core: 2. Of those that a mesh axis runs over, the one named last changes fastest.
Arguments:
- pixels: float32 [224, 128, 1024], P('ba', 'gy', 'gx'), may hold values from -8 to 8
- spectra: float32 [224, 256], P('ba'), may hold values from -0.375 to 0.375
- abundance: float32 [256, 128, 1024], P('ba', 'gy', 'gx'), may hold values from 0 to 1
- plan: int32 [3], replicated, may hold values from 0 to 1, as said below
Outputs:
- sparse: float32 [256, 128, 1024], P('ba', 'gy', 'gx')
- spectra_grad: float32 [224, 256], P('ba')
The draws below stay inside these ranges and needn't reach their ends.
Inputs may be any that keep to these rules, and one draw needn't show every extreme that they name: `plan`: entry 0 is 1 and at least one later entry is 0.
All inputs are finite; a program needn't handle non-finite values. Where the reference program divides by a largest or mean magnitude, that divisor is 1e-20 or more.
Results may differ from the reference program's by a relative error of at most 0.0001.
Values sent between devices are 32-bit elements; how exact they have to be, the bound alone decides.
No kernel may reach another device: no remote copies, remote signals or barrier semaphores. Data moves between devices by JAX's collectives and lax.ppermute only.
A program may use at most 64 MiB of HBM per device.

```python
import math
import jax
import jax.numpy as jnp
from jax import lax

L = 224
P_SIZE = 256
SWEEPS = 3
NR = 128
NC = 1024


def draw_pixels(key, part):
    frac_c = jnp.arange(NC, dtype=jnp.float32) / max(NC - 1, 1)
    frac_r = jnp.arange(NR, dtype=jnp.float32) / max(NR - 1, 1)
    row_scale = 0.5 * jnp.power(3.0, frac_r)
    values = jax.random.normal(key, (L, NR, NC), jnp.float32)
    col_scale = 0.6 * jnp.power(3.0, frac_c)
    scale = row_scale[:, None] * col_scale[None, :]
    return jnp.clip(values * scale[None, :, :], -8.0, 8.0).astype(jnp.float32)


def draw_abundance(key, part):
    frac_c = jnp.arange(NC, dtype=jnp.float32) / max(NC - 1, 1)
    frac_r = jnp.arange(NR, dtype=jnp.float32) / max(NR - 1, 1)
    frac_p = jnp.arange(P_SIZE, dtype=jnp.float32) / max(P_SIZE - 1, 1)
    values = jax.random.uniform(key, (P_SIZE, NR, NC), jnp.float32, 0.0, 1.0)
    col_scale = 0.3 * jnp.power(1.0 / 0.3, frac_c)
    row_scale = 0.3 * jnp.power(1.0 / 0.3, frac_r)
    comp_scale = 0.5 * jnp.power(2.0, frac_p)
    scale = comp_scale[:, None, None] * row_scale[None, :, None] * col_scale[None, None, :]
    return jnp.clip(values * scale, 0.0, 1.0).astype(jnp.float32)


def draw_plan(key, part):
    flips = jax.random.randint(key, (SWEEPS,), 0, 2)
    zero_at = jax.random.randint(jax.random.fold_in(key, 7), (), 1, SWEEPS)
    places = jnp.arange(SWEEPS)
    flips = jnp.where(places == zero_at, 0, flips)
    return jnp.where(places == 0, 1, flips).astype(jnp.int32)


def block_levels(stream_key, extent, pieces, low, largest):
    gain, own = 1.0, jax.random.fold_in(stream_key, 6)
    for axis_at, parts in pieces:
        steps = jnp.exp(jax.random.uniform(jax.random.fold_in(own, axis_at), (parts,), jnp.float32, low / len(pieces), largest / len(pieces)))
        gain = gain * jnp.repeat(steps, extent[axis_at] // parts).reshape([-1 if axis == axis_at else 1 for axis in range(len(extent))])
    return gain


def scatter_about(key, extent, deviation, reach, shards=(), held_as=jnp.bfloat16):
    drawn = deviation * jax.random.normal(key, extent, jnp.float32)
    if shards:
        drawn = drawn * block_levels(key, extent, shards, -0.22, 0.18)
    return jnp.clip(drawn, -reach, reach).astype(held_as)


def setup_inputs(seed: int = 0) -> dict:
    streams_of = jax.random.split(jax.random.key(seed), 5)
    pixels = draw_pixels(jax.random.fold_in(streams_of[4], 71), 0)
    spectra = scatter_about(streams_of[1], (L, P_SIZE), P_SIZE ** -0.5, 0.375, ((0, 4),), jnp.float32)
    abundance = draw_abundance(jax.random.fold_in(streams_of[4], 71), 0)
    plan = draw_plan(jax.random.fold_in(streams_of[4], 71), 0)
    return {"pixels": pixels, "spectra": spectra, "abundance": abundance, "plan": plan}


HIGHEST = lax.Precision.HIGHEST
penalty = 1.0
tv_weight = 0.2
sparsity = 0.05

def from_left(values):
    return jnp.pad(values, ((0, 0), (0, 0), (1, 0)))[:, :, :-1]

def from_above(values):
    return jnp.pad(values, ((0, 0), (1, 0), (0, 0)))[:, :-1, :]

def reference(pixels, spectra, abundance, plan):
    gram = jnp.dot(spectra.T, spectra, precision=HIGHEST)
    bound = jnp.max(lax.optimization_barrier(jnp.sum(jnp.abs(gram), axis=1)))
    rows_ok = (jnp.arange(NR) < NR - 1).astype(jnp.float32)[None, :, None]
    cols_ok = (jnp.arange(NC) < NC - 1).astype(jnp.float32)[None, None, :]
    field = abundance
    sparse = abundance
    dual = jnp.zeros_like(abundance)
    weight = jnp.ones_like(abundance)
    for sweep in range(SWEEPS):
        padded = jnp.pad(field, ((0, 0), (0, 1), (0, 1)))
        diff_h = (padded[:, :-1, 1:] - field) * cols_ok
        diff_v = (padded[:, 1:, :-1] - field) * rows_ok
        energy = diff_h * diff_h + diff_v * diff_v
        smooth_sq = jnp.sum(energy) / (P_SIZE * NR * NC) + 1e-06
        fresh = 1.0 / jnp.sqrt(energy + smooth_sq)
        weight = jnp.where(plan[sweep] == 1, fresh, weight)
        flux_h = weight * diff_h
        flux_v = weight * diff_v
        edge_h = weight * cols_ok
        edge_v = weight * rows_ok
        tv_grad = from_left(flux_h) - flux_h + from_above(flux_v) - flux_v
        degree = edge_h + from_left(edge_h) + edge_v + from_above(edge_v)
        resid = jnp.einsum('lp,prc->lrc', spectra, field, precision=HIGHEST) - pixels
        data_grad = jnp.einsum('lp,lrc->prc', spectra, resid, precision=HIGHEST)
        grad_total = data_grad + tv_weight * tv_grad + penalty * (field - sparse + dual)
        field = field - grad_total / (bound + penalty + 2.0 * tv_weight * degree)
        sparse = jnp.maximum(field + dual - sparsity / penalty, 0.0)
        dual = dual + field - sparse
    resid = jnp.einsum('lp,prc->lrc', spectra, sparse, precision=HIGHEST) - pixels
    spectra_grad = jnp.einsum('lrc,prc->lp', resid, sparse, precision=HIGHEST) / math.sqrt(NR * NC)
    return (sparse, spectra_grad)
```

```python
import math

import jax
import jax.numpy as jnp
from jax import lax
from jax.sharding import PartitionSpec as P

SWEEPS = 3


HIGHEST = lax.Precision.HIGHEST
penalty = 1.0
tv_weight = 0.2
sparsity = 0.05

ROWS = ("gy", "ba")


def extended_2(x, sides, width):
    for axis, size, dim in sides:
        length = x.shape[dim]
        up = [(i, i + 1) for i in range(size - 1)]
        down = [(j, i) for i, j in up]
        last = lax.slice_in_dim(x, length - width, length, axis=dim)
        leading = lax.slice_in_dim(x, 0, width, axis=dim)
        before = lax.ppermute(last, axis, up)
        after = lax.ppermute(leading, axis, down)
        x = jnp.concatenate([before, x, after], axis=dim)
    return x


def edge_masks(top_row, left_col, row_count, col_count, grid_rows, grid_cols):
    ext_rows = top_row - 1 + jnp.arange(row_count + 1)
    ext_cols = left_col - 1 + jnp.arange(col_count + 1)
    rows_in = (ext_rows >= 0) & (ext_rows <= grid_rows - 1)
    cols_in = (ext_cols >= 0) & (ext_cols <= grid_cols - 1)
    rows_ok = (ext_rows >= 0) & (ext_rows <= grid_rows - 2)
    cols_ok = (ext_cols >= 0) & (ext_cols <= grid_cols - 2)
    mask_h = (rows_in[:, None] & cols_ok[None, :]).astype(jnp.float32)[None]
    mask_v = (rows_ok[:, None] & cols_in[None, :]).astype(jnp.float32)[None]
    return (mask_h, mask_v)


def total_of(x, axes=("ba", "gy", "gx")):
    for axis in axes:
        x = lax.psum(x, axis)
    return x


def local(pixels, spectra, abundance, plan):
    band_ways = lax.axis_size("ba")
    row_ways = lax.axis_size("gy") * band_ways
    field = lax.all_to_all(abundance, "ba", 1, 0, tiled=True)
    bands = lax.all_to_all(pixels, "ba", 1, 0, tiled=True)
    all_comps, row_count, gx_cols = field.shape
    grid_rows = row_count * row_ways
    grid_cols = gx_cols * lax.axis_size("gx")
    row_block = lax.axis_index("gy") * band_ways + lax.axis_index("ba")
    top_row = row_block * row_count
    all_spectra = lax.all_gather(spectra, "ba", axis=0, tiled=True)
    gram = jnp.dot(all_spectra.T, all_spectra, precision=HIGHEST)
    bound = jnp.max(jnp.sum(jnp.abs(gram), axis=1))
    left_col = lax.axis_index("gx") * gx_cols
    mask_h, mask_v = edge_masks(top_row, left_col, row_count, gx_cols, grid_rows, grid_cols)
    sparse = field
    dual = jnp.zeros_like(field)
    weight = jnp.ones((all_comps, row_count + 1, gx_cols + 1), jnp.float32)
    for sweep in range(SWEEPS):
        extended = extended_2(field, (("gx", lax.axis_size("gx"), 2), (ROWS, row_ways, 1)), 1)
        center = extended[:, : row_count + 1, : gx_cols + 1]
        right = extended[:, : row_count + 1, 1:]
        below = extended[:, 1:, : gx_cols + 1]
        diff_h = (right - center) * mask_h
        diff_v = (below - center) * mask_v
        energy = diff_h * diff_h + diff_v * diff_v
        total = total_of(jnp.sum(energy[:, 1:, 1:]))
        smooth_sq = total / (all_comps * grid_rows * grid_cols) + 1e-06
        fresh = 1.0 / jnp.sqrt(energy + smooth_sq)
        weight = jnp.where(plan[sweep] == 1, fresh, weight)
        flux_h = weight * diff_h
        flux_v = weight * diff_v
        edge_h = weight * mask_h
        edge_v = weight * mask_v
        tv_grad = flux_h[:, 1:, :-1] - flux_h[:, 1:, 1:] + flux_v[:, :-1, 1:] - flux_v[:, 1:, 1:]
        degree = edge_h[:, 1:, 1:] + edge_h[:, 1:, :-1] + edge_v[:, 1:, 1:] + edge_v[:, :-1, 1:]
        resid = jnp.einsum("lq,qrc->lrc", all_spectra, field, precision=HIGHEST) - bands
        data_grad = jnp.einsum("lp,lrc->prc", all_spectra, resid, precision=HIGHEST)
        grad_total = data_grad + tv_weight * tv_grad + penalty * (field - sparse + dual)
        field = field - grad_total / (bound + penalty + 2.0 * tv_weight * degree)
        sparse = jnp.maximum(field + dual - sparsity / penalty, 0.0)
        dual = dual + field - sparse
    resid = jnp.einsum("lp,prc->lrc", all_spectra, sparse, precision=HIGHEST) - bands
    partial_grad = jnp.einsum("lrc,prc->lp", resid, sparse, precision=HIGHEST) / math.sqrt(
        grid_rows * grid_cols
    )
    spectra_grad = lax.psum_scatter(partial_grad, "ba", scatter_dimension=0, tiled=True)
    spectra_grad = total_of(spectra_grad, ("gx", "gy"))
    out = lax.all_to_all(sparse, "ba", 0, 1, tiled=True)
    return (out, spectra_grad)


def solution(mesh):
    return jax.shard_map(
        local,
        mesh=mesh,
        in_specs=(P("ba", "gy", "gx"), P("ba", None), P("ba", "gy", "gx"), P()),
        out_specs=(P("ba", "gy", "gx"), P("ba", None)),
        check_vma=False,
    )
```

```python
import math

import jax
import jax.numpy as jnp
from jax import lax
from jax.sharding import PartitionSpec as P

SWEEPS = 3


HIGHEST = lax.Precision.HIGHEST
penalty = 1.0
tv_weight = 0.2
sparsity = 0.05

ROWS = ("gy", "ba")


def extended_2(x, sides, width):
    for axis, size, dim in sides:
        length = x.shape[dim]
        up = [(i, i + 1) for i in range(size - 1)]
        down = [(j, i) for i, j in up]
        last = lax.slice_in_dim(x, length - width, length, axis=dim)
        leading = lax.slice_in_dim(x, 0, width, axis=dim)
        before = lax.ppermute(last, axis, up)
        after = lax.ppermute(leading, axis, down)
        x = jnp.concatenate([before, x, after], axis=dim)
    return x


def edge_masks(top_row, left_col, row_count, col_count, grid_rows, grid_cols):
    ext_rows = top_row - 1 + jnp.arange(row_count + 1)
    ext_cols = left_col - 1 + jnp.arange(col_count + 1)
    rows_in = (ext_rows >= 0) & (ext_rows <= grid_rows - 1)
    cols_in = (ext_cols >= 0) & (ext_cols <= grid_cols - 1)
    rows_ok = (ext_rows >= 0) & (ext_rows <= grid_rows - 2)
    cols_ok = (ext_cols >= 0) & (ext_cols <= grid_cols - 2)
    mask_h = (rows_in[:, None] & cols_ok[None, :]).astype(jnp.float32)[None]
    mask_v = (rows_ok[:, None] & cols_in[None, :]).astype(jnp.float32)[None]
    return (mask_h, mask_v)


def total_of(x, axes=("ba", "gy", "gx")):
    for axis in axes:
        size = lax.axis_size(axis)
        step = 1
        while step < size:
            x = x + lax.ppermute(x, axis, [(i, i ^ step) for i in range(size)])
            step *= 2
    return x


def local(pixels, spectra, abundance, plan):
    band_ways = lax.axis_size("ba")
    row_ways = lax.axis_size("gy") * band_ways
    field = lax.all_to_all(abundance, "ba", 1, 0, tiled=True)
    bands = lax.all_to_all(pixels, "ba", 1, 0, tiled=True)
    all_comps, row_count, gx_cols = field.shape
    grid_rows = row_count * row_ways
    grid_cols = gx_cols * lax.axis_size("gx")
    row_block = lax.axis_index("gy") * band_ways + lax.axis_index("ba")
    top_row = row_block * row_count
    all_spectra = lax.all_gather(spectra, "ba", axis=0, tiled=True)
    gram = jnp.dot(all_spectra.T, all_spectra, precision=HIGHEST)
    bound = jnp.max(jnp.sum(jnp.abs(gram), axis=1))
    left_col = lax.axis_index("gx") * gx_cols
    mask_h, mask_v = edge_masks(top_row, left_col, row_count, gx_cols, grid_rows, grid_cols)
    sparse = field
    dual = jnp.zeros_like(field)
    weight = jnp.ones((all_comps, row_count + 1, gx_cols + 1), jnp.float32)
    for sweep in range(SWEEPS):
        extended = extended_2(field, (("gx", lax.axis_size("gx"), 2), (ROWS, row_ways, 1)), 1)
        center = extended[:, : row_count + 1, : gx_cols + 1]
        right = extended[:, : row_count + 1, 1:]
        below = extended[:, 1:, : gx_cols + 1]
        diff_h = (right - center) * mask_h
        diff_v = (below - center) * mask_v
        energy = diff_h * diff_h + diff_v * diff_v
        total = total_of(jnp.sum(energy[:, 1:, 1:]))
        smooth_sq = total / (all_comps * grid_rows * grid_cols) + 1e-06
        fresh = 1.0 / jnp.sqrt(energy + smooth_sq)
        weight = jnp.where(plan[sweep] == 1, fresh, weight)
        flux_h = weight * diff_h
        flux_v = weight * diff_v
        edge_h = weight * mask_h
        edge_v = weight * mask_v
        tv_grad = flux_h[:, 1:, :-1] - flux_h[:, 1:, 1:] + flux_v[:, :-1, 1:] - flux_v[:, 1:, 1:]
        degree = edge_h[:, 1:, 1:] + edge_h[:, 1:, :-1] + edge_v[:, 1:, 1:] + edge_v[:, :-1, 1:]
        resid = jnp.einsum("lq,qrc->lrc", all_spectra, field, precision=HIGHEST) - bands
        data_grad = jnp.einsum("lp,lrc->prc", all_spectra, resid, precision=HIGHEST)
        grad_total = data_grad + tv_weight * tv_grad + penalty * (field - sparse + dual)
        field = field - grad_total / (bound + penalty + 2.0 * tv_weight * degree)
        sparse = jnp.maximum(field + dual - sparsity / penalty, 0.0)
        dual = dual + field - sparse
    resid = jnp.einsum("lp,prc->lrc", all_spectra, sparse, precision=HIGHEST) - bands
    partial_grad = jnp.einsum("lrc,prc->lp", resid, sparse, precision=HIGHEST) / math.sqrt(
        grid_rows * grid_cols
    )
    spectra_grad = lax.psum_scatter(partial_grad, "ba", scatter_dimension=0, tiled=True)
    spectra_grad = total_of(spectra_grad, ("gx", "gy"))
    out = lax.all_to_all(sparse, "ba", 0, 1, tiled=True)
    return (out, spectra_grad)


def solution(mesh):
    return jax.shard_map(
        local,
        mesh=mesh,
        in_specs=(P("ba", "gy", "gx"), P("ba", None), P("ba", "gy", "gx"), P()),
        out_specs=(P("ba", "gy", "gx"), P("ba", None)),
        check_vma=False,
    )
```

```python
import math

import jax
import jax.numpy as jnp
from jax import lax
from jax.sharding import PartitionSpec as P

SWEEPS = 3


HIGHEST = lax.Precision.HIGHEST
penalty = 1.0
tv_weight = 0.2
sparsity = 0.05

ROWS = ("gy", "ba")


def extended_2(x, sides, width):
    for axis, size, dim in sides:
        length = x.shape[dim]
        up = [(i, i + 1) for i in range(size - 1)]
        down = [(j, i) for i, j in up]
        last = lax.slice_in_dim(x, length - width, length, axis=dim)
        leading = lax.slice_in_dim(x, 0, width, axis=dim)
        before = lax.ppermute(last, axis, up)
        after = lax.ppermute(leading, axis, down)
        x = jnp.concatenate([before, x, after], axis=dim)
    return x


def edge_masks(top_row, left_col, row_count, col_count, grid_rows, grid_cols):
    ext_rows = top_row - 1 + jnp.arange(row_count + 1)
    ext_cols = left_col - 1 + jnp.arange(col_count + 1)
    rows_in = (ext_rows >= 0) & (ext_rows <= grid_rows - 1)
    cols_in = (ext_cols >= 0) & (ext_cols <= grid_cols - 1)
    rows_ok = (ext_rows >= 0) & (ext_rows <= grid_rows - 2)
    cols_ok = (ext_cols >= 0) & (ext_cols <= grid_cols - 2)
    mask_h = (rows_in[:, None] & cols_ok[None, :]).astype(jnp.float32)[None]
    mask_v = (rows_ok[:, None] & cols_in[None, :]).astype(jnp.float32)[None]
    return (mask_h, mask_v)


def from_all(x, axis):
    size, me = lax.axis_size(axis), lax.axis_index(axis)
    got = [x] + [
        lax.ppermute(x, axis, [(i, (i + shift) % size) for i in range(size)])
        for shift in range(1, size)
    ]
    return jnp.stack(got)[(me - jnp.arange(size)) % size]


def total_of(x, axes=("ba", "gy", "gx")):
    for axis in axes:
        x = jnp.sum(from_all(x, axis), axis=0)
    return x


def scatter_total(x, axis):
    size, me = lax.axis_size(axis), lax.axis_index(axis)
    block = x.shape[0] // size
    got = [lax.dynamic_slice_in_dim(x, me * block, block, 0)]
    for shift in range(1, size):
        part = lax.dynamic_slice_in_dim(x, ((me + shift) % size) * block, block, 0)
        got.append(lax.ppermute(part, axis, [(i, (i + shift) % size) for i in range(size)]))
    return jnp.sum(jnp.stack(got)[(me - jnp.arange(size)) % size], axis=0)


def local(pixels, spectra, abundance, plan):
    band_ways = lax.axis_size("ba")
    row_ways = lax.axis_size("gy") * band_ways
    field = lax.all_to_all(abundance, "ba", 1, 0, tiled=True)
    bands = lax.all_to_all(pixels, "ba", 1, 0, tiled=True)
    all_comps, row_count, gx_cols = field.shape
    grid_rows = row_count * row_ways
    grid_cols = gx_cols * lax.axis_size("gx")
    row_block = lax.axis_index("gy") * band_ways + lax.axis_index("ba")
    top_row = row_block * row_count
    all_spectra = lax.all_gather(spectra, "ba", axis=0, tiled=True)
    gram = jnp.dot(all_spectra.T, all_spectra, precision=HIGHEST)
    bound = jnp.max(jnp.sum(jnp.abs(gram), axis=1))
    left_col = lax.axis_index("gx") * gx_cols
    mask_h, mask_v = edge_masks(top_row, left_col, row_count, gx_cols, grid_rows, grid_cols)
    sparse = field
    dual = jnp.zeros_like(field)
    weight = jnp.ones((all_comps, row_count + 1, gx_cols + 1), jnp.float32)

    def sweep_of(sweep, carry):
        field, sparse, dual, weight = carry
        extended = extended_2(field, (("gx", lax.axis_size("gx"), 2), (ROWS, row_ways, 1)), 1)
        center = extended[:, : row_count + 1, : gx_cols + 1]
        right = extended[:, : row_count + 1, 1:]
        below = extended[:, 1:, : gx_cols + 1]
        diff_h = (right - center) * mask_h
        diff_v = (below - center) * mask_v
        energy = diff_h * diff_h + diff_v * diff_v
        total = total_of(jnp.sum(energy[:, 1:, 1:]))
        smooth_sq = total / (all_comps * grid_rows * grid_cols) + 1e-06
        fresh = 1.0 / jnp.sqrt(energy + smooth_sq)
        weight = jnp.where(plan[sweep] == 1, fresh, weight)
        flux_h = weight * diff_h
        flux_v = weight * diff_v
        edge_h = weight * mask_h
        edge_v = weight * mask_v
        tv_grad = flux_h[:, 1:, :-1] - flux_h[:, 1:, 1:] + flux_v[:, :-1, 1:] - flux_v[:, 1:, 1:]
        degree = edge_h[:, 1:, 1:] + edge_h[:, 1:, :-1] + edge_v[:, 1:, 1:] + edge_v[:, :-1, 1:]
        resid = jnp.einsum("lq,qrc->lrc", all_spectra, field, precision=HIGHEST) - bands
        data_grad = jnp.einsum("lp,lrc->prc", all_spectra, resid, precision=HIGHEST)
        grad_total = data_grad + tv_weight * tv_grad + penalty * (field - sparse + dual)
        field = field - grad_total / (bound + penalty + 2.0 * tv_weight * degree)
        sparse = jnp.maximum(field + dual - sparsity / penalty, 0.0)
        dual = dual + field - sparse
        return (field, sparse, dual, weight)

    field, sparse, dual, weight = lax.fori_loop(0, SWEEPS, sweep_of, (field, sparse, dual, weight))
    resid = jnp.einsum("lp,prc->lrc", all_spectra, sparse, precision=HIGHEST) - bands
    partial_grad = jnp.einsum("lrc,prc->lp", resid, sparse, precision=HIGHEST) / math.sqrt(
        grid_rows * grid_cols
    )
    spectra_grad = scatter_total(partial_grad, "ba")
    spectra_grad = total_of(spectra_grad, ("gx", "gy"))
    out = lax.all_to_all(sparse, "ba", 0, 1, tiled=True)
    return (out, spectra_grad)


def solution(mesh):
    return jax.shard_map(
        local,
        mesh=mesh,
        in_specs=(P("ba", "gy", "gx"), P("ba", None), P("ba", "gy", "gx"), P()),
        out_specs=(P("ba", "gy", "gx"), P("ba", None)),
        check_vma=False,
    )
```

```python
import math

import jax
import jax.numpy as jnp
from jax import lax
from jax.sharding import PartitionSpec as P

SWEEPS = 3


HIGHEST = lax.Precision.HIGHEST
penalty = 1.0
tv_weight = 0.2
sparsity = 0.05

ROWS = ("gy", "ba")


def extended_2(x, sides, width):
    for axis, size, dim in sides:
        length = x.shape[dim]
        up = [(i, i + 1) for i in range(size - 1)]
        down = [(j, i) for i, j in up]
        last = lax.slice_in_dim(x, length - width, length, axis=dim)
        leading = lax.slice_in_dim(x, 0, width, axis=dim)
        before = lax.ppermute(last, axis, up)
        after = lax.ppermute(leading, axis, down)
        x = jnp.concatenate([before, x, after], axis=dim)
    return x


def edge_masks(top_row, left_col, row_count, col_count, grid_rows, grid_cols):
    ext_rows = top_row - 1 + jnp.arange(row_count + 1)
    ext_cols = left_col - 1 + jnp.arange(col_count + 1)
    rows_in = (ext_rows >= 0) & (ext_rows <= grid_rows - 1)
    cols_in = (ext_cols >= 0) & (ext_cols <= grid_cols - 1)
    rows_ok = (ext_rows >= 0) & (ext_rows <= grid_rows - 2)
    cols_ok = (ext_cols >= 0) & (ext_cols <= grid_cols - 2)
    mask_h = (rows_in[:, None] & cols_ok[None, :]).astype(jnp.float32)[None]
    mask_v = (rows_ok[:, None] & cols_in[None, :]).astype(jnp.float32)[None]
    return (mask_h, mask_v)


def total_of(x, axes=("ba", "gy", "gx")):
    for axis in axes:
        size = lax.axis_size(axis)
        step = 1
        while step < size:
            x = x + lax.ppermute(x, axis, [(i, i ^ step) for i in range(size)])
            step *= 2
    return x


def local(pixels, spectra, abundance, plan):
    band_ways = lax.axis_size("ba")
    row_ways = lax.axis_size("gy") * band_ways
    field = lax.all_to_all(abundance, "ba", 1, 0, tiled=True)
    bands = lax.all_to_all(pixels, "ba", 1, 0, tiled=True)
    all_comps, row_count, gx_cols = field.shape
    grid_rows = row_count * row_ways
    grid_cols = gx_cols * lax.axis_size("gx")
    row_block = lax.axis_index("gy") * band_ways + lax.axis_index("ba")
    top_row = row_block * row_count
    all_spectra = lax.all_gather(spectra, "ba", axis=0, tiled=True)
    gram = jnp.dot(all_spectra.T, all_spectra, precision=HIGHEST)
    bound = jnp.max(jnp.sum(jnp.abs(gram), axis=1))
    left_col = lax.axis_index("gx") * gx_cols
    mask_h, mask_v = edge_masks(top_row, left_col, row_count, gx_cols, grid_rows, grid_cols)
    sparse = field
    dual = jnp.zeros_like(field)
    weight = jnp.ones((all_comps, row_count + 1, gx_cols + 1), jnp.float32)
    for sweep in range(SWEEPS):
        extended = extended_2(field, (("gx", lax.axis_size("gx"), 2), (ROWS, row_ways, 1)), 1)
        center = extended[:, : row_count + 1, : gx_cols + 1]
        right = extended[:, : row_count + 1, 1:]
        below = extended[:, 1:, : gx_cols + 1]
        diff_h = (right - center) * mask_h
        diff_v = (below - center) * mask_v

        def refreshed(diff_h, diff_v, weight):
            energy = diff_h * diff_h + diff_v * diff_v
            total = total_of(jnp.sum(energy[:, 1:, 1:]))
            smooth_sq = total / (all_comps * grid_rows * grid_cols) + 1e-06
            return 1.0 / jnp.sqrt(energy + smooth_sq)

        def kept(diff_h, diff_v, weight):
            return weight

        if sweep == 0:
            weight = refreshed(diff_h, diff_v, weight)
        else:
            weight = lax.cond(plan[sweep] == 1, refreshed, kept, diff_h, diff_v, weight)
        flux_h = weight * diff_h
        flux_v = weight * diff_v
        edge_h = weight * mask_h
        edge_v = weight * mask_v
        tv_grad = flux_h[:, 1:, :-1] - flux_h[:, 1:, 1:] + flux_v[:, :-1, 1:] - flux_v[:, 1:, 1:]
        degree = edge_h[:, 1:, 1:] + edge_h[:, 1:, :-1] + edge_v[:, 1:, 1:] + edge_v[:, :-1, 1:]
        resid = jnp.einsum("lq,qrc->lrc", all_spectra, field, precision=HIGHEST) - bands
        data_grad = jnp.einsum("lp,lrc->prc", all_spectra, resid, precision=HIGHEST)
        grad_total = data_grad + tv_weight * tv_grad + penalty * (field - sparse + dual)
        field = field - grad_total / (bound + penalty + 2.0 * tv_weight * degree)
        sparse = jnp.maximum(field + dual - sparsity / penalty, 0.0)
        dual = dual + field - sparse
    resid = jnp.einsum("lp,prc->lrc", all_spectra, sparse, precision=HIGHEST) - bands
    partial_grad = jnp.einsum("lrc,prc->lp", resid, sparse, precision=HIGHEST) / math.sqrt(
        grid_rows * grid_cols
    )
    spectra_grad = lax.psum_scatter(partial_grad, "ba", scatter_dimension=0, tiled=True)
    spectra_grad = total_of(spectra_grad, ("gx", "gy"))
    out = lax.all_to_all(sparse, "ba", 0, 1, tiled=True)
    return (out, spectra_grad)


def solution(mesh):
    return jax.shard_map(
        local,
        mesh=mesh,
        in_specs=(P("ba", "gy", "gx"), P("ba", None), P("ba", "gy", "gx"), P()),
        out_specs=(P("ba", "gy", "gx"), P("ba", None)),
        check_vma=False,
    )
```

```python
import math

import jax
import jax.numpy as jnp
from jax import lax
from jax.sharding import PartitionSpec as P

SWEEPS = 3


HIGHEST = lax.Precision.HIGHEST
penalty = 1.0
tv_weight = 0.2
sparsity = 0.05

ROWS = ("gy", "ba")


def shifted(x, axes, size, offset):
    pairs = [(i, i + offset) for i in range(size) if 0 <= i + offset < size]
    return lax.ppermute(x, axes, pairs)


def shifted_2(x, axes, sizes, offsets):
    (n0, n1), (d0, d1) = sizes, offsets
    pairs = [
        (i * n1 + j, (i + d0) * n1 + j + d1)
        for i in range(n0)
        for j in range(n1)
        if 0 <= i + d0 < n0 and 0 <= j + d1 < n1
    ]
    return lax.ppermute(x, axes, pairs)


def extended_1(x, col_axis, col_ways, row_axes, row_ways):
    comps, rows, cols = x.shape
    both = (col_axis,) + row_axes
    both_ways = (col_ways, row_ways)
    up = shifted(x[:, rows - 1 :, :], row_axes, row_ways, 1)
    down = shifted(x[:, :1, :], row_axes, row_ways, -1)
    left = shifted(x[:, :, cols - 1 :], col_axis, col_ways, 1)
    right = shifted(x[:, :, :1], col_axis, col_ways, -1)
    top_right = shifted_2(x[:, rows - 1 :, :1], both, both_ways, (-1, 1))
    bottom_left = shifted_2(x[:, :1, cols - 1 :], both, both_ways, (1, -1))
    pad = jnp.zeros((comps, 1, 1), x.dtype)
    top = jnp.concatenate([pad, up, top_right], axis=2)
    middle = jnp.concatenate([left, x, right], axis=2)
    bottom = jnp.concatenate([bottom_left, down, pad], axis=2)
    return jnp.concatenate([top, middle, bottom], axis=1)


def edge_masks(top_row, left_col, row_count, col_count, grid_rows, grid_cols):
    ext_rows = top_row - 1 + jnp.arange(row_count + 1)
    ext_cols = left_col - 1 + jnp.arange(col_count + 1)
    rows_in = (ext_rows >= 0) & (ext_rows <= grid_rows - 1)
    cols_in = (ext_cols >= 0) & (ext_cols <= grid_cols - 1)
    rows_ok = (ext_rows >= 0) & (ext_rows <= grid_rows - 2)
    cols_ok = (ext_cols >= 0) & (ext_cols <= grid_cols - 2)
    mask_h = (rows_in[:, None] & cols_ok[None, :]).astype(jnp.float32)[None]
    mask_v = (rows_ok[:, None] & cols_in[None, :]).astype(jnp.float32)[None]
    return (mask_h, mask_v)


def total_of(x, axes=("ba", "gy", "gx")):
    for axis in axes:
        size = lax.axis_size(axis)
        step = 1
        while step < size:
            x = x + lax.ppermute(x, axis, [(i, i ^ step) for i in range(size)])
            step *= 2
    return x


def total_everywhere(x):
    axes = ("gx", "gy", "ba")
    size = 1
    for axis in axes:
        size *= lax.axis_size(axis)
    return jnp.sum(lax.all_to_all(jnp.broadcast_to(x, (size,)), axes, 0, 0, tiled=True))


def local(pixels, spectra, abundance, plan):
    band_ways = lax.axis_size("ba")
    row_ways = lax.axis_size("gy") * band_ways
    field = lax.all_to_all(abundance, "ba", 1, 0, tiled=True)
    bands = lax.all_to_all(pixels, "ba", 1, 0, tiled=True)
    all_comps, row_count, gx_cols = field.shape
    grid_rows = row_count * row_ways
    grid_cols = gx_cols * lax.axis_size("gx")
    row_block = lax.axis_index("gy") * band_ways + lax.axis_index("ba")
    top_row = row_block * row_count
    all_spectra = lax.all_gather(spectra, "ba", axis=0, tiled=True)
    gram = jnp.dot(all_spectra.T, all_spectra, precision=HIGHEST)
    bound = jnp.max(jnp.sum(jnp.abs(gram), axis=1))
    left_col = lax.axis_index("gx") * gx_cols
    mask_h, mask_v = edge_masks(top_row, left_col, row_count, gx_cols, grid_rows, grid_cols)
    sparse = field
    dual = jnp.zeros_like(field)
    weight = jnp.ones((all_comps, row_count + 1, gx_cols + 1), jnp.float32)
    for sweep in range(SWEEPS):
        extended = extended_1(field, "gx", lax.axis_size("gx"), ROWS, row_ways)
        center = extended[:, : row_count + 1, : gx_cols + 1]
        right = extended[:, : row_count + 1, 1:]
        below = extended[:, 1:, : gx_cols + 1]
        diff_h = (right - center) * mask_h
        diff_v = (below - center) * mask_v

        energy = diff_h * diff_h + diff_v * diff_v
        local_total = jnp.sum(energy[:, 1:, 1:])
        if sweep == 0:
            total = total_everywhere(local_total)
        else:
            total = lax.cond(plan[sweep] == 1, total_everywhere, lambda x: x, local_total)
        smooth_sq = total / (all_comps * grid_rows * grid_cols) + 1e-06
        fresh = 1.0 / jnp.sqrt(energy + smooth_sq)
        weight = fresh if sweep == 0 else jnp.where(plan[sweep] == 1, fresh, weight)
        flux_h = weight * diff_h
        flux_v = weight * diff_v
        edge_h = weight * mask_h
        edge_v = weight * mask_v
        tv_grad = flux_h[:, 1:, :-1] - flux_h[:, 1:, 1:] + flux_v[:, :-1, 1:] - flux_v[:, 1:, 1:]
        degree = edge_h[:, 1:, 1:] + edge_h[:, 1:, :-1] + edge_v[:, 1:, 1:] + edge_v[:, :-1, 1:]
        resid = jnp.einsum("lq,qrc->lrc", all_spectra, field, precision=HIGHEST) - bands
        data_grad = jnp.einsum("lp,lrc->prc", all_spectra, resid, precision=HIGHEST)
        grad_total = data_grad + tv_weight * tv_grad + penalty * (field - sparse + dual)
        field = field - grad_total / (bound + penalty + 2.0 * tv_weight * degree)
        sparse = jnp.maximum(field + dual - sparsity / penalty, 0.0)
        dual = dual + field - sparse
    resid = jnp.einsum("lp,prc->lrc", all_spectra, sparse, precision=HIGHEST) - bands
    partial_grad = jnp.einsum("lrc,prc->lp", resid, sparse, precision=HIGHEST) / math.sqrt(
        grid_rows * grid_cols
    )
    spectra_grad = lax.psum_scatter(partial_grad, "ba", scatter_dimension=0, tiled=True)
    spectra_grad = total_of(spectra_grad, ("gx", "gy"))
    out = lax.all_to_all(sparse, "ba", 0, 1, tiled=True)
    return (out, spectra_grad)


def solution(mesh):
    return jax.shard_map(
        local,
        mesh=mesh,
        in_specs=(P("ba", "gy", "gx"), P("ba", None), P("ba", "gy", "gx"), P()),
        out_specs=(P("ba", "gy", "gx"), P("ba", None)),
        check_vma=False,
    )
```

```python
import math

import jax
import jax.numpy as jnp
from jax import lax
from jax.sharding import PartitionSpec as P

SWEEPS = 3


HIGHEST = lax.Precision.HIGHEST
penalty = 1.0
tv_weight = 0.2
sparsity = 0.05

ROWS = ("gy", "ba")


def shifted(x, axes, size, offset):
    pairs = [(i, i + offset) for i in range(size) if 0 <= i + offset < size]
    return lax.ppermute(x, axes, pairs)


def shifted_2(x, axes, sizes, offsets):
    (n0, n1), (d0, d1) = sizes, offsets
    pairs = [
        (i * n1 + j, (i + d0) * n1 + j + d1)
        for i in range(n0)
        for j in range(n1)
        if 0 <= i + d0 < n0 and 0 <= j + d1 < n1
    ]
    return lax.ppermute(x, axes, pairs)


def extended_1(x, col_axis, col_ways, row_axes, row_ways):
    comps, rows, cols = x.shape
    both = (col_axis,) + row_axes
    both_ways = (col_ways, row_ways)
    up = shifted(x[:, rows - 1 :, :], row_axes, row_ways, 1)
    down = shifted(x[:, :1, :], row_axes, row_ways, -1)
    left = shifted(x[:, :, cols - 1 :], col_axis, col_ways, 1)
    right = shifted(x[:, :, :1], col_axis, col_ways, -1)
    top_right = shifted_2(x[:, rows - 1 :, :1], both, both_ways, (-1, 1))
    bottom_left = shifted_2(x[:, :1, cols - 1 :], both, both_ways, (1, -1))
    pad = jnp.zeros((comps, 1, 1), x.dtype)
    top = jnp.concatenate([pad, up, top_right], axis=2)
    middle = jnp.concatenate([left, x, right], axis=2)
    bottom = jnp.concatenate([bottom_left, down, pad], axis=2)
    return jnp.concatenate([top, middle, bottom], axis=1)


def edge_masks(top_row, left_col, row_count, col_count, grid_rows, grid_cols):
    ext_rows = top_row - 1 + jnp.arange(row_count + 1)
    ext_cols = left_col - 1 + jnp.arange(col_count + 1)
    rows_in = (ext_rows >= 0) & (ext_rows <= grid_rows - 1)
    cols_in = (ext_cols >= 0) & (ext_cols <= grid_cols - 1)
    rows_ok = (ext_rows >= 0) & (ext_rows <= grid_rows - 2)
    cols_ok = (ext_cols >= 0) & (ext_cols <= grid_cols - 2)
    mask_h = (rows_in[:, None] & cols_ok[None, :]).astype(jnp.float32)[None]
    mask_v = (rows_ok[:, None] & cols_in[None, :]).astype(jnp.float32)[None]
    return (mask_h, mask_v)


def total_of(x, axes=("ba", "gy", "gx")):
    for axis in axes:
        size = lax.axis_size(axis)
        step = 1
        while step < size:
            x = x + lax.ppermute(x, axis, [(i, i ^ step) for i in range(size)])
            step *= 2
    return x


def total_everywhere(x):
    axes = ("gx", "gy", "ba")
    size = 1
    for axis in axes:
        size *= lax.axis_size(axis)
    return jnp.sum(lax.all_to_all(jnp.broadcast_to(x, (size,)), axes, 0, 0, tiled=True))


def scatter_everywhere(x, axes):
    size = 1
    for axis in axes:
        size *= lax.axis_size(axis)
    parts = x.reshape((size, -1))
    return jnp.sum(lax.all_to_all(parts[:, None], axes, 0, 1, tiled=True)[0], axis=0)


def gathered(x, axes):
    size = 1
    for axis in axes:
        size *= lax.axis_size(axis)
    spread = jnp.broadcast_to(x[None], (size,) + x.shape)
    return lax.all_to_all(spread, axes, 0, 0, tiled=True)


def local(pixels, spectra, abundance, plan):
    band_ways = lax.axis_size("ba")
    row_ways = lax.axis_size("gy") * band_ways
    field = lax.all_to_all(abundance, "ba", 1, 0, tiled=True)
    bands = lax.all_to_all(pixels, "ba", 1, 0, tiled=True)
    all_comps, row_count, gx_cols = field.shape
    grid_rows = row_count * row_ways
    grid_cols = gx_cols * lax.axis_size("gx")
    row_block = lax.axis_index("gy") * band_ways + lax.axis_index("ba")
    top_row = row_block * row_count
    all_spectra = gathered(spectra, ("ba",)).reshape((-1,) + spectra.shape[1:])
    gram = jnp.dot(all_spectra.T, all_spectra, precision=HIGHEST)
    bound = jnp.max(jnp.sum(jnp.abs(gram), axis=1))
    left_col = lax.axis_index("gx") * gx_cols
    mask_h, mask_v = edge_masks(top_row, left_col, row_count, gx_cols, grid_rows, grid_cols)
    sparse = field
    dual = jnp.zeros_like(field)
    weight = jnp.ones((all_comps, row_count + 1, gx_cols + 1), jnp.float32)
    for sweep in range(SWEEPS):
        extended = extended_1(field, "gx", lax.axis_size("gx"), ROWS, row_ways)
        center = extended[:, : row_count + 1, : gx_cols + 1]
        right = extended[:, : row_count + 1, 1:]
        below = extended[:, 1:, : gx_cols + 1]
        diff_h = (right - center) * mask_h
        diff_v = (below - center) * mask_v

        energy = diff_h * diff_h + diff_v * diff_v
        local_total = jnp.sum(energy[:, 1:, 1:])
        if sweep == 0:
            total = total_everywhere(local_total)
        else:
            total = lax.cond(plan[sweep] == 1, total_everywhere, lambda x: x, local_total)
        smooth_sq = total / (all_comps * grid_rows * grid_cols) + 1e-06
        fresh = 1.0 / jnp.sqrt(energy + smooth_sq)
        weight = fresh if sweep == 0 else jnp.where(plan[sweep] == 1, fresh, weight)
        flux_h = weight * diff_h
        flux_v = weight * diff_v
        edge_h = weight * mask_h
        edge_v = weight * mask_v
        tv_grad = flux_h[:, 1:, :-1] - flux_h[:, 1:, 1:] + flux_v[:, :-1, 1:] - flux_v[:, 1:, 1:]
        degree = edge_h[:, 1:, 1:] + edge_h[:, 1:, :-1] + edge_v[:, 1:, 1:] + edge_v[:, :-1, 1:]
        resid = jnp.einsum("lq,qrc->lrc", all_spectra, field, precision=HIGHEST) - bands
        data_grad = jnp.einsum("lp,lrc->prc", all_spectra, resid, precision=HIGHEST)
        grad_total = data_grad + tv_weight * tv_grad + penalty * (field - sparse + dual)
        field = field - grad_total / (bound + penalty + 2.0 * tv_weight * degree)
        sparse = jnp.maximum(field + dual - sparsity / penalty, 0.0)
        dual = dual + field - sparse
    resid = jnp.einsum("lp,prc->lrc", all_spectra, sparse, precision=HIGHEST) - bands
    partial_grad = jnp.einsum("lrc,prc->lp", resid, sparse, precision=HIGHEST) / math.sqrt(
        grid_rows * grid_cols
    )
    block = scatter_everywhere(partial_grad, ("ba", "gx", "gy"))
    spectra_grad = gathered(block, ("gx", "gy")).reshape((-1,) + partial_grad.shape[1:])
    out = lax.all_to_all(sparse, "ba", 0, 1, tiled=True)
    return (out, spectra_grad)


def solution(mesh):
    return jax.shard_map(
        local,
        mesh=mesh,
        in_specs=(P("ba", "gy", "gx"), P("ba", None), P("ba", "gy", "gx"), P()),
        out_specs=(P("ba", "gy", "gx"), P("ba", None)),
        check_vma=False,
    )
```

```python
import math

import jax
import jax.numpy as jnp
from jax import lax
from jax.sharding import PartitionSpec as P

SWEEPS = 3


HIGHEST = lax.Precision.HIGHEST
penalty = 1.0
tv_weight = 0.2
sparsity = 0.05

ROWS = ("gy", "ba")


def shifted(x, axes, size, offset):
    pairs = [(i, i + offset) for i in range(size) if 0 <= i + offset < size]
    return lax.ppermute(x, axes, pairs)


def shifted_2(x, axes, sizes, offsets):
    (n0, n1), (d0, d1) = sizes, offsets
    pairs = [
        (i * n1 + j, (i + d0) * n1 + j + d1)
        for i in range(n0)
        for j in range(n1)
        if 0 <= i + d0 < n0 and 0 <= j + d1 < n1
    ]
    return lax.ppermute(x, axes, pairs)


def extended_1(x, col_axis, col_ways, row_axes, row_ways):
    comps, rows, cols = x.shape
    both = (col_axis,) + row_axes
    both_ways = (col_ways, row_ways)
    up = shifted(x[:, rows - 1 :, :], row_axes, row_ways, 1)
    down = shifted(x[:, :1, :], row_axes, row_ways, -1)
    left = shifted(x[:, :, cols - 1 :], col_axis, col_ways, 1)
    right = shifted(x[:, :, :1], col_axis, col_ways, -1)
    top_right = shifted_2(x[:, rows - 1 :, :1], both, both_ways, (-1, 1))
    bottom_left = shifted_2(x[:, :1, cols - 1 :], both, both_ways, (1, -1))
    pad = jnp.zeros((comps, 1, 1), x.dtype)
    top = jnp.concatenate([pad, up, top_right], axis=2)
    middle = jnp.concatenate([left, x, right], axis=2)
    bottom = jnp.concatenate([bottom_left, down, pad], axis=2)
    return jnp.concatenate([top, middle, bottom], axis=1)


def edge_masks(top_row, left_col, row_count, col_count, grid_rows, grid_cols):
    ext_rows = top_row - 1 + jnp.arange(row_count + 1)
    ext_cols = left_col - 1 + jnp.arange(col_count + 1)
    rows_in = (ext_rows >= 0) & (ext_rows <= grid_rows - 1)
    cols_in = (ext_cols >= 0) & (ext_cols <= grid_cols - 1)
    rows_ok = (ext_rows >= 0) & (ext_rows <= grid_rows - 2)
    cols_ok = (ext_cols >= 0) & (ext_cols <= grid_cols - 2)
    mask_h = (rows_in[:, None] & cols_ok[None, :]).astype(jnp.float32)[None]
    mask_v = (rows_ok[:, None] & cols_in[None, :]).astype(jnp.float32)[None]
    return (mask_h, mask_v)


def total_of(x, axes=("ba", "gy", "gx")):
    for axis in axes:
        size = lax.axis_size(axis)
        step = 1
        while step < size:
            x = x + lax.ppermute(x, axis, [(i, i ^ step) for i in range(size)])
            step *= 2
    return x


def total_everywhere(x):
    axes = ("gx", "gy", "ba")
    size = 1
    for axis in axes:
        size *= lax.axis_size(axis)
    return jnp.sum(lax.all_to_all(jnp.broadcast_to(x, (size,)), axes, 0, 0, tiled=True))


def scatter_everywhere(x, axes):
    size = 1
    for axis in axes:
        size *= lax.axis_size(axis)
    parts = x.reshape((size, -1))
    return jnp.sum(lax.all_to_all(parts[:, None], axes, 0, 1, tiled=True)[0], axis=0)


def gathered(x, axes):
    size = 1
    for axis in axes:
        size *= lax.axis_size(axis)
    spread = jnp.broadcast_to(x[None], (size,) + x.shape)
    return lax.all_to_all(spread, axes, 0, 0, tiled=True)


def local(pixels, spectra, abundance, plan):
    band_ways = lax.axis_size("ba")
    row_ways = lax.axis_size("gy") * band_ways
    comps, bands_here = abundance.shape[0], pixels.shape[0]
    rows_here, cols_here = abundance.shape[1:]
    quarter = rows_here // band_ways
    lines = spectra.shape[1] // cols_here
    copy = jnp.zeros((bands_here, quarter, cols_here), spectra.dtype)
    copy = copy.at[:, :lines].set(spectra.reshape(bands_here, lines, cols_here))
    sent = jnp.concatenate([abundance, pixels, jnp.tile(copy, (1, band_ways, 1))], axis=0)
    got = lax.all_to_all(sent, "ba", 1, 0, tiled=True).reshape(
        (band_ways, comps + 2 * bands_here, quarter, cols_here)
    )
    field = got[:, :comps].reshape((band_ways * comps, quarter, cols_here))
    bands = got[:, comps : comps + bands_here].reshape((band_ways * bands_here, quarter, cols_here))
    all_spectra = got[:, comps + bands_here :, :lines].reshape((band_ways * bands_here, -1))
    all_comps, row_count, gx_cols = field.shape
    grid_rows = row_count * row_ways
    grid_cols = gx_cols * lax.axis_size("gx")
    row_block = lax.axis_index("gy") * band_ways + lax.axis_index("ba")
    top_row = row_block * row_count
    gram = jnp.dot(all_spectra.T, all_spectra, precision=HIGHEST)
    bound = jnp.max(jnp.sum(jnp.abs(gram), axis=1))
    left_col = lax.axis_index("gx") * gx_cols
    mask_h, mask_v = edge_masks(top_row, left_col, row_count, gx_cols, grid_rows, grid_cols)
    sparse = field
    dual = jnp.zeros_like(field)
    weight = jnp.ones((all_comps, row_count + 1, gx_cols + 1), jnp.float32)
    for sweep in range(SWEEPS):
        extended = extended_1(field, "gx", lax.axis_size("gx"), ROWS, row_ways)
        center = extended[:, : row_count + 1, : gx_cols + 1]
        right = extended[:, : row_count + 1, 1:]
        below = extended[:, 1:, : gx_cols + 1]
        diff_h = (right - center) * mask_h
        diff_v = (below - center) * mask_v

        energy = diff_h * diff_h + diff_v * diff_v
        local_total = jnp.sum(energy[:, 1:, 1:])
        if sweep == 0:
            total = total_everywhere(local_total)
        else:
            total = lax.cond(plan[sweep] == 1, total_everywhere, lambda x: x, local_total)
        smooth_sq = total / (all_comps * grid_rows * grid_cols) + 1e-06
        fresh = 1.0 / jnp.sqrt(energy + smooth_sq)
        weight = fresh if sweep == 0 else jnp.where(plan[sweep] == 1, fresh, weight)
        flux_h = weight * diff_h
        flux_v = weight * diff_v
        edge_h = weight * mask_h
        edge_v = weight * mask_v
        tv_grad = flux_h[:, 1:, :-1] - flux_h[:, 1:, 1:] + flux_v[:, :-1, 1:] - flux_v[:, 1:, 1:]
        degree = edge_h[:, 1:, 1:] + edge_h[:, 1:, :-1] + edge_v[:, 1:, 1:] + edge_v[:, :-1, 1:]
        resid = jnp.einsum("lq,qrc->lrc", all_spectra, field, precision=HIGHEST) - bands
        data_grad = jnp.einsum("lp,lrc->prc", all_spectra, resid, precision=HIGHEST)
        grad_total = data_grad + tv_weight * tv_grad + penalty * (field - sparse + dual)
        field = field - grad_total / (bound + penalty + 2.0 * tv_weight * degree)
        sparse = jnp.maximum(field + dual - sparsity / penalty, 0.0)
        dual = dual + field - sparse
    resid = jnp.einsum("lp,prc->lrc", all_spectra, sparse, precision=HIGHEST) - bands
    partial_grad = jnp.einsum("lrc,prc->lp", resid, sparse, precision=HIGHEST) / math.sqrt(
        grid_rows * grid_cols
    )
    block = scatter_everywhere(partial_grad, ("ba", "gx", "gy"))
    spectra_grad = gathered(block, ("gx", "gy")).reshape((-1,) + partial_grad.shape[1:])
    out = lax.all_to_all(sparse, "ba", 0, 1, tiled=True)
    return (out, spectra_grad)


def solution(mesh):
    return jax.shard_map(
        local,
        mesh=mesh,
        in_specs=(P("ba", "gy", "gx"), P("ba", None), P("ba", "gy", "gx"), P()),
        out_specs=(P("ba", "gy", "gx"), P("ba", None)),
        check_vma=False,
    )
```

```python
import math

import jax
import jax.numpy as jnp
from jax import lax
from jax.sharding import PartitionSpec as P

SWEEPS = 3


HIGHEST = lax.Precision.HIGHEST
penalty = 1.0
tv_weight = 0.2
sparsity = 0.05

ROWS = ("gy", "ba")


def shifted(x, axes, size, offset):
    pairs = [(i, i + offset) for i in range(size) if 0 <= i + offset < size]
    return lax.ppermute(x, axes, pairs)


def shifted_2(x, axes, sizes, offsets):
    (n0, n1), (d0, d1) = sizes, offsets
    pairs = [
        (i * n1 + j, (i + d0) * n1 + j + d1)
        for i in range(n0)
        for j in range(n1)
        if 0 <= i + d0 < n0 and 0 <= j + d1 < n1
    ]
    return lax.ppermute(x, axes, pairs)


def extended_1(x, col_axis, col_ways, row_axes, row_ways):
    comps, rows, cols = x.shape
    both = (col_axis,) + row_axes
    both_ways = (col_ways, row_ways)
    up = shifted(x[:, rows - 1 :, :], row_axes, row_ways, 1)
    down = shifted(x[:, :1, :], row_axes, row_ways, -1)
    left = shifted(x[:, :, cols - 1 :], col_axis, col_ways, 1)
    right = shifted(x[:, :, :1], col_axis, col_ways, -1)
    top_right = shifted_2(x[:, rows - 1 :, :1], both, both_ways, (-1, 1))
    bottom_left = shifted_2(x[:, :1, cols - 1 :], both, both_ways, (1, -1))
    pad = jnp.zeros((comps, 1, 1), x.dtype)
    top = jnp.concatenate([pad, up, top_right], axis=2)
    middle = jnp.concatenate([left, x, right], axis=2)
    bottom = jnp.concatenate([bottom_left, down, pad], axis=2)
    return jnp.concatenate([top, middle, bottom], axis=1)


def edge_masks(top_row, left_col, row_count, col_count, grid_rows, grid_cols):
    ext_rows = top_row - 1 + jnp.arange(row_count + 1)
    ext_cols = left_col - 1 + jnp.arange(col_count + 1)
    rows_in = (ext_rows >= 0) & (ext_rows <= grid_rows - 1)
    cols_in = (ext_cols >= 0) & (ext_cols <= grid_cols - 1)
    rows_ok = (ext_rows >= 0) & (ext_rows <= grid_rows - 2)
    cols_ok = (ext_cols >= 0) & (ext_cols <= grid_cols - 2)
    mask_h = (rows_in[:, None] & cols_ok[None, :]).astype(jnp.float32)[None]
    mask_v = (rows_ok[:, None] & cols_in[None, :]).astype(jnp.float32)[None]
    return (mask_h, mask_v)


def total_of(x, axes=("ba", "gy", "gx")):
    for axis in axes:
        size = lax.axis_size(axis)
        step = 1
        while step < size:
            x = x + lax.ppermute(x, axis, [(i, i ^ step) for i in range(size)])
            step *= 2
    return x


def total_everywhere(x):
    axes = ("gx", "gy", "ba")
    size = 1
    for axis in axes:
        size *= lax.axis_size(axis)
    return jnp.sum(lax.all_to_all(jnp.broadcast_to(x, (size,)), axes, 0, 0, tiled=True))


def scatter_everywhere(x, axes):
    size = 1
    for axis in axes:
        size *= lax.axis_size(axis)
    parts = x.reshape((size, -1))
    return jnp.sum(lax.all_to_all(parts[:, None], axes, 0, 1, tiled=True)[0], axis=0)


def gathered(x, axes):
    size = 1
    for axis in axes:
        size *= lax.axis_size(axis)
    spread = jnp.broadcast_to(x[None], (size,) + x.shape)
    return lax.all_to_all(spread, axes, 0, 0, tiled=True)


def local(pixels, spectra, abundance, plan):
    band_ways = lax.axis_size("ba")
    row_ways = lax.axis_size("gy") * band_ways
    field = lax.all_to_all(abundance, "ba", 1, 0, tiled=True)
    bands = lax.all_to_all(pixels, "ba", 1, 0, tiled=True)
    all_comps, row_count, gx_cols = field.shape
    grid_rows = row_count * row_ways
    grid_cols = gx_cols * lax.axis_size("gx")
    row_block = lax.axis_index("gy") * band_ways + lax.axis_index("ba")
    top_row = row_block * row_count
    all_spectra = gathered(spectra, ("ba",)).reshape((-1,) + spectra.shape[1:])
    gram = jnp.dot(all_spectra.T, all_spectra, precision=HIGHEST)
    bound = jnp.max(jnp.sum(jnp.abs(gram), axis=1))
    left_col = lax.axis_index("gx") * gx_cols
    mask_h, mask_v = edge_masks(top_row, left_col, row_count, gx_cols, grid_rows, grid_cols)
    sparse = field
    dual = jnp.zeros_like(field)
    weight = jnp.ones((all_comps, row_count + 1, gx_cols + 1), jnp.float32)
    for sweep in range(SWEEPS):
        extended = extended_1(field, "gx", lax.axis_size("gx"), ROWS, row_ways)
        center = extended[:, : row_count + 1, : gx_cols + 1]
        right = extended[:, : row_count + 1, 1:]
        below = extended[:, 1:, : gx_cols + 1]
        diff_h = (right - center) * mask_h
        diff_v = (below - center) * mask_v

        energy = diff_h * diff_h + diff_v * diff_v
        local_total = jnp.sum(energy[:, 1:, 1:])
        if sweep == 0:
            total = total_everywhere(local_total)
        else:
            total = lax.cond(plan[sweep] == 1, total_everywhere, lambda x: x, local_total)
        smooth_sq = total / (all_comps * grid_rows * grid_cols) + 1e-06
        fresh = 1.0 / jnp.sqrt(energy + smooth_sq)
        weight = fresh if sweep == 0 else jnp.where(plan[sweep] == 1, fresh, weight)
        flux_h = weight * diff_h
        flux_v = weight * diff_v
        edge_h = weight * mask_h
        edge_v = weight * mask_v
        tv_grad = flux_h[:, 1:, :-1] - flux_h[:, 1:, 1:] + flux_v[:, :-1, 1:] - flux_v[:, 1:, 1:]
        degree = edge_h[:, 1:, 1:] + edge_h[:, 1:, :-1] + edge_v[:, 1:, 1:] + edge_v[:, :-1, 1:]
        resid = jnp.einsum("lq,qrc->lrc", all_spectra, field, precision=HIGHEST) - bands
        data_grad = jnp.einsum("lp,lrc->prc", all_spectra, resid, precision=HIGHEST)
        grad_total = data_grad + tv_weight * tv_grad + penalty * (field - sparse + dual)
        field = field - grad_total / (bound + penalty + 2.0 * tv_weight * degree)
        sparse = jnp.maximum(field + dual - sparsity / penalty, 0.0)
        dual = dual + field - sparse
    resid = jnp.einsum("lp,prc->lrc", all_spectra, sparse, precision=HIGHEST) - bands
    partial_grad = jnp.einsum("lrc,prc->lp", resid, sparse, precision=HIGHEST) / math.sqrt(
        grid_rows * grid_cols
    )
    comps = all_comps // band_ways
    quarter_cols = row_count * gx_cols
    lines = partial_grad.size // (band_ways * quarter_cols)
    sent = jnp.concatenate(
        [
            sparse.reshape((band_ways, comps, row_count, gx_cols)),
            partial_grad.reshape((band_ways, lines, row_count, gx_cols)),
        ],
        axis=1,
    )
    got = lax.all_to_all(sent, "ba", 0, 0, tiled=True)
    out = got[:, :comps].transpose((1, 0, 2, 3)).reshape((comps, band_ways * row_count, gx_cols))
    own_bands = jnp.sum(got[:, comps:].reshape((band_ways, -1, partial_grad.shape[1])), axis=0)
    block = scatter_everywhere(own_bands, ("gx", "gy"))
    spectra_grad = gathered(block, ("gx", "gy")).reshape(own_bands.shape)
    return (out, spectra_grad)


def solution(mesh):
    return jax.shard_map(
        local,
        mesh=mesh,
        in_specs=(P("ba", "gy", "gx"), P("ba", None), P("ba", "gy", "gx"), P()),
        out_specs=(P("ba", "gy", "gx"), P("ba", None)),
        check_vma=False,
    )
```

```python
import math

import jax
import jax.numpy as jnp
from jax import lax
from jax.sharding import PartitionSpec as P

SWEEPS = 3


HIGHEST = lax.Precision.HIGHEST
penalty = 1.0
tv_weight = 0.2
sparsity = 0.05

ROWS = ("gy", "ba")


def shifted(x, axes, size, offset):
    pairs = [(i, i + offset) for i in range(size) if 0 <= i + offset < size]
    return lax.ppermute(x, axes, pairs)


def shifted_2(x, axes, sizes, offsets):
    (n0, n1), (d0, d1) = sizes, offsets
    pairs = [
        (i * n1 + j, (i + d0) * n1 + j + d1)
        for i in range(n0)
        for j in range(n1)
        if 0 <= i + d0 < n0 and 0 <= j + d1 < n1
    ]
    return lax.ppermute(x, axes, pairs)


def extended_1(x, col_axis, col_ways, row_axes, row_ways):
    comps, rows, cols = x.shape
    both = (col_axis,) + row_axes
    both_ways = (col_ways, row_ways)
    up = shifted(x[:, rows - 1 :, :], row_axes, row_ways, 1)
    down = shifted(x[:, :1, :], row_axes, row_ways, -1)
    left = shifted(x[:, :, cols - 1 :], col_axis, col_ways, 1)
    right = shifted(x[:, :, :1], col_axis, col_ways, -1)
    top_right = shifted_2(x[:, rows - 1 :, :1], both, both_ways, (-1, 1))
    bottom_left = shifted_2(x[:, :1, cols - 1 :], both, both_ways, (1, -1))
    pad = jnp.zeros((comps, 1, 1), x.dtype)
    top = jnp.concatenate([pad, up, top_right], axis=2)
    middle = jnp.concatenate([left, x, right], axis=2)
    bottom = jnp.concatenate([bottom_left, down, pad], axis=2)
    return jnp.concatenate([top, middle, bottom], axis=1)


def edge_masks(top_row, left_col, row_count, col_count, grid_rows, grid_cols):
    ext_rows = top_row - 1 + jnp.arange(row_count + 1)
    ext_cols = left_col - 1 + jnp.arange(col_count + 1)
    rows_in = (ext_rows >= 0) & (ext_rows <= grid_rows - 1)
    cols_in = (ext_cols >= 0) & (ext_cols <= grid_cols - 1)
    rows_ok = (ext_rows >= 0) & (ext_rows <= grid_rows - 2)
    cols_ok = (ext_cols >= 0) & (ext_cols <= grid_cols - 2)
    mask_h = (rows_in[:, None] & cols_ok[None, :]).astype(jnp.float32)[None]
    mask_v = (rows_ok[:, None] & cols_in[None, :]).astype(jnp.float32)[None]
    return (mask_h, mask_v)


def total_of(x, axes=("ba", "gy", "gx")):
    for axis in axes:
        size = lax.axis_size(axis)
        step = 1
        while step < size:
            x = x + lax.ppermute(x, axis, [(i, i ^ step) for i in range(size)])
            step *= 2
    return x


def total_everywhere(x):
    axes = ("gx", "gy", "ba")
    size = 1
    for axis in axes:
        size *= lax.axis_size(axis)
    return jnp.sum(lax.all_to_all(jnp.broadcast_to(x, (size,)), axes, 0, 0, tiled=True))


def scatter_everywhere(x, axes):
    size = 1
    for axis in axes:
        size *= lax.axis_size(axis)
    parts = x.reshape((size, -1))
    return jnp.sum(lax.all_to_all(parts[:, None], axes, 0, 1, tiled=True)[0], axis=0)


def gathered(x, axes):
    size = 1
    for axis in axes:
        size *= lax.axis_size(axis)
    spread = jnp.broadcast_to(x[None], (size,) + x.shape)
    return lax.all_to_all(spread, axes, 0, 0, tiled=True)


def local(pixels, spectra, abundance, plan):
    band_ways = lax.axis_size("ba")
    row_ways = lax.axis_size("gy") * band_ways
    field = lax.all_to_all(abundance, "ba", 1, 0, tiled=True)
    bands = lax.all_to_all(pixels, "ba", 1, 0, tiled=True)
    all_comps, row_count, gx_cols = field.shape
    grid_rows = row_count * row_ways
    grid_cols = gx_cols * lax.axis_size("gx")
    row_block = lax.axis_index("gy") * band_ways + lax.axis_index("ba")
    top_row = row_block * row_count
    all_spectra = gathered(spectra, ("ba",)).reshape((-1,) + spectra.shape[1:])
    gram = jnp.dot(all_spectra.T, all_spectra, precision=HIGHEST)
    bound = jnp.max(jnp.sum(jnp.abs(gram), axis=1))
    left_col = lax.axis_index("gx") * gx_cols
    mask_h, mask_v = edge_masks(top_row, left_col, row_count, gx_cols, grid_rows, grid_cols)
    sparse = field
    dual = jnp.zeros_like(field)
    weight = jnp.ones((all_comps, row_count + 1, gx_cols + 1), jnp.float32)
    for sweep in range(SWEEPS):
        extended = extended_1(field, "gx", lax.axis_size("gx"), ROWS, row_ways)
        center = extended[:, : row_count + 1, : gx_cols + 1]
        right = extended[:, : row_count + 1, 1:]
        below = extended[:, 1:, : gx_cols + 1]
        diff_h = (right - center) * mask_h
        diff_v = (below - center) * mask_v

        energy = diff_h * diff_h + diff_v * diff_v
        local_total = jnp.sum(energy[:, 1:, 1:])
        if sweep == 0:
            total = total_everywhere(local_total)
        else:
            total = lax.cond(plan[sweep] == 1, total_everywhere, lambda x: x, local_total)
        smooth_sq = total / (all_comps * grid_rows * grid_cols) + 1e-06
        fresh = 1.0 / jnp.sqrt(energy + smooth_sq)
        weight = fresh if sweep == 0 else jnp.where(plan[sweep] == 1, fresh, weight)
        flux_h = weight * diff_h
        flux_v = weight * diff_v
        edge_h = weight * mask_h
        edge_v = weight * mask_v
        tv_grad = flux_h[:, 1:, :-1] - flux_h[:, 1:, 1:] + flux_v[:, :-1, 1:] - flux_v[:, 1:, 1:]
        degree = edge_h[:, 1:, 1:] + edge_h[:, 1:, :-1] + edge_v[:, 1:, 1:] + edge_v[:, :-1, 1:]
        resid = jnp.einsum("lq,qrc->lrc", all_spectra, field, precision=HIGHEST) - bands
        data_grad = jnp.einsum("lp,lrc->prc", all_spectra, resid, precision=HIGHEST)
        grad_total = data_grad + tv_weight * tv_grad + penalty * (field - sparse + dual)
        field = field - grad_total / (bound + penalty + 2.0 * tv_weight * degree)
        sparse = jnp.maximum(field + dual - sparsity / penalty, 0.0)
        dual = dual + field - sparse
    resid = jnp.einsum("lp,prc->lrc", all_spectra, sparse, precision=HIGHEST) - bands
    partial_grad = jnp.einsum("lrc,prc->lp", resid, sparse, precision=HIGHEST) / math.sqrt(
        grid_rows * grid_cols
    )
    comps = all_comps // band_ways
    quarter_cols = row_count * gx_cols
    lines = partial_grad.size // (band_ways * quarter_cols)
    sent = jnp.concatenate(
        [
            sparse.reshape((band_ways, comps, row_count, gx_cols)),
            partial_grad.reshape((band_ways, lines, row_count, gx_cols)),
        ],
        axis=1,
    )
    got = lax.all_to_all(sent, "ba", 0, 0, tiled=True)
    out = got[:, :comps].transpose((1, 0, 2, 3)).reshape((comps, band_ways * row_count, gx_cols))
    own_bands = jnp.sum(got[:, comps:].reshape((band_ways, -1, partial_grad.shape[1])), axis=0)
    spectra_grad = total_of(own_bands, ("gx", "gy"))
    return (out, spectra_grad)


def solution(mesh):
    return jax.shard_map(
        local,
        mesh=mesh,
        in_specs=(P("ba", "gy", "gx"), P("ba", None), P("ba", "gy", "gx"), P()),
        out_specs=(P("ba", "gy", "gx"), P("ba", None)),
        check_vma=False,
    )
```
